256 devices in a mesh: sector: 64 (over z, y, core), dof: 4 (over x).
Axes of the slice: x: 4, y: 4, z: 8, core: 2. Of those that a mesh axis runs over, the one named last changes fastest.
Arguments:
- load_history: bfloat16 [64, 64, 6144], P('sector', None, 'dof'), may hold values from -6 to 6
- sector_basis: bfloat16 [6144, 1536], P('dof'), may hold values from -0.078125 to 0.078125
- harmonic_modes: bfloat16 [64, 1536, 256], P('sector'), may hold values from -0.15625 to 0.15625
- stress_basis: bfloat16 [1536, 6144], P(None, 'dof'), may hold values from -0.375 to 0.375
- mode_decay: float32 [64, 256], P('sector'), may hold values from 0.01 to 0.3
- mode_phase: float32 [64, 256], P('sector'), may hold values from 0.05 to 1.5
- mode_count: int32 [64], P('sector'), may hold values from 64 to 256, as said below
- slot_harmonic: int32 [64], replicated, may hold values from 0 to 63, each once
Outputs:
- stress_field: bfloat16 [64, 64, 6144], P('sector', None, 'dof')
The draws below stay inside these ranges and needn't reach their ends.
Inputs may be any that keep to these rules, and one draw needn't show every extreme that they name: Slot modes from mode_count on are left out; some slot has 256 live modes and some 256 // 4. `slot_harmonic`: every harmonic component is held by exactly one slot.
All inputs are finite; a program needn't handle non-finite values.
Results may differ from the reference program's by a relative error of at most 0.025.
Values may be sent and summed in bfloat16 or wider, within the bound.
No kernel may reach another device: no remote copies, remote signals or barrier semaphores. Data moves between devices by JAX's collectives and lax.ppermute only.
A program may use at most 64 MiB of HBM per device.

```python
import math
import jax
import jax.numpy as jnp
from jax import lax

STEPS = 64
REDUCED = 1536
MODES = 256
SECTORS = 64
DOFS = 6144
STRESS = 6144


def draw_mode_count(key, part):
    key_values, key_top, key_low = jax.random.split(key, 3)
    counts = jax.random.randint(key_values, (SECTORS,), MODES // 4, MODES + 1, dtype=jnp.int32)
    top_slot = jax.random.randint(key_top, (), 0, SECTORS, dtype=jnp.int32)
    step_away = jax.random.randint(key_low, (), 1, SECTORS, dtype=jnp.int32)
    low_slot = (top_slot + step_away) % SECTORS
    counts = counts.at[top_slot].set(MODES)
    counts = counts.at[low_slot].set(MODES // 4)
    return counts


def steps_of(own_key, extent, shards, smallest, largest):
    factor_of, own = 1.0, jax.random.fold_in(own_key, 6)
    for dim, parts in shards:
        heights = jnp.exp(jax.random.uniform(jax.random.fold_in(own, dim), (parts,), jnp.float32, smallest / len(shards), largest / len(shards)))
        factor_of = factor_of * jnp.repeat(heights, extent[dim] // parts).reshape([-1 if axis == dim else 1 for axis in range(len(extent))])
    return factor_of


def gaussian(rng, extent, deviation, most, cuts=(), held_as=jnp.bfloat16):
    values = jax.random.normal(rng, extent, jnp.float32) * deviation
    if len(cuts) > 0:
        values = steps_of(rng, extent, cuts, -0.22, 0.18) * values
    return jnp.clip(values, min=-most, max=most).astype(held_as)


def setup_inputs(seed: int = 0) -> dict:
    streams_of = jax.random.split(jax.random.key(seed), 9)
    load_history = gaussian(streams_of[0], (SECTORS, STEPS, DOFS), 1.0, 6.0, ((0, 64), (2, 4)))
    sector_basis = gaussian(streams_of[1], (DOFS, REDUCED), DOFS ** -0.5, 0.078125, ((0, 4),))
    harmonic_modes = gaussian(streams_of[2], (SECTORS, REDUCED, MODES), REDUCED ** -0.5, 0.15625, ((0, 64),))
    stress_basis = gaussian(streams_of[3], (REDUCED, STRESS), MODES ** -0.5, 0.375, ((1, 4),))
    mode_decay = jnp.clip(jnp.exp(math.log(0.3) - 3.4011974 * jax.random.uniform(streams_of[4], (SECTORS, MODES), jnp.float32) ** steps_of(streams_of[4], (SECTORS, MODES), ((0, 64),), -0.2, 0.2)), 0.01, 0.3)
    mode_phase = jnp.clip(0.05 + 1.45 * jax.random.uniform(streams_of[5], (SECTORS, MODES), jnp.float32) ** steps_of(streams_of[5], (SECTORS, MODES), ((0, 64),), -0.2, 0.2), 0.05, 1.5)
    mode_count = draw_mode_count(jax.random.fold_in(streams_of[8], 71), 0)
    slot_harmonic = jax.random.permutation(streams_of[7], SECTORS).astype(jnp.int32)
    return dict(load_history=load_history, sector_basis=sector_basis, harmonic_modes=harmonic_modes, stress_basis=stress_basis, mode_decay=mode_decay, mode_phase=mode_phase, mode_count=mode_count, slot_harmonic=slot_harmonic)


def transform_table(slot_harmonic):
    count_all = slot_harmonic.shape[0]
    half_count = count_all // 2
    sine_rows = slot_harmonic > half_count
    harmonic_order = jnp.where(sine_rows, slot_harmonic - half_count, slot_harmonic).astype(jnp.int32)
    sector_index = jnp.arange(count_all, dtype=jnp.int32)
    residue = harmonic_order[:, None] * sector_index[None, :] % count_all
    phase_angle = residue.astype(jnp.float32) * jnp.float32(2.0 * math.pi / count_all)
    wave_table = jnp.where(sine_rows[:, None], jnp.sin(phase_angle), jnp.cos(phase_angle))
    single = (slot_harmonic == 0) | (slot_harmonic == half_count)
    weight = jnp.where(single, jnp.float32(1.0 / count_all), jnp.float32(2.0 / count_all))
    return jnp.sqrt(weight)[:, None] * wave_table

def filter_kernel(decay_rates, phase_steps, steps_count):
    time_index = jnp.arange(steps_count, dtype=jnp.int32)
    offset = time_index[:, None] - time_index[None, :]
    causal = offset >= 0
    lag_value = jnp.maximum(offset, 0).astype(jnp.float32)
    gain_factor = jnp.sqrt(1.0 - jnp.exp(-2.0 * decay_rates))
    shape_table = gain_factor[..., None, None] * jnp.exp(-decay_rates[..., None, None] * lag_value) * jnp.cos(phase_steps[..., None, None] * lag_value)
    return jnp.where(causal, shape_table, jnp.float32(0.0))

def reference(load_history, sector_basis, harmonic_modes, stress_basis, mode_decay, mode_phase, mode_count, slot_harmonic):
    highest = lax.Precision.HIGHEST
    table = transform_table(slot_harmonic)
    count_all, steps_count, rows_all = load_history.shape
    flat_loads = load_history.reshape(count_all * steps_count, rows_all).astype(jnp.float32)
    reduced = jnp.dot(flat_loads, sector_basis.astype(jnp.float32), precision=highest)
    reduced = lax.optimization_barrier(reduced.astype(jnp.bfloat16)).reshape(count_all, steps_count, -1)
    spectrum = jnp.einsum('ks,stc->ktc', table, reduced.astype(jnp.float32), precision=highest)
    spectrum = lax.optimization_barrier(spectrum.astype(jnp.bfloat16))
    modes_wide = harmonic_modes.astype(jnp.float32)
    modal = jnp.einsum('ktc,kcm->ktm', spectrum.astype(jnp.float32), modes_wide, precision=highest)
    live = jnp.arange(harmonic_modes.shape[2], dtype=jnp.int32)[None, :] < mode_count[:, None]
    modal = modal * live[:, None, :].astype(jnp.float32)
    kernel = filter_kernel(mode_decay, mode_phase, steps_count)
    response = jnp.einsum('kmtu,kum->ktm', kernel, modal, precision=highest)
    response = lax.optimization_barrier(response.astype(jnp.bfloat16))
    returned = jnp.einsum('ktm,kcm->ktc', response.astype(jnp.float32), modes_wide, precision=highest)
    returned = lax.optimization_barrier(returned.astype(jnp.bfloat16))
    back = jnp.einsum('ks,ktc->stc', table, returned.astype(jnp.float32), precision=highest)
    back = lax.optimization_barrier(back.astype(jnp.bfloat16))
    flat_back = back.reshape(count_all * steps_count, -1).astype(jnp.float32)
    stress_field = jnp.dot(flat_back, stress_basis.astype(jnp.float32), precision=highest)
    return stress_field.astype(jnp.bfloat16).reshape(count_all, steps_count, -1)
```

```python
import math

import jax
import jax.numpy as jnp
from jax import lax
from jax.sharding import PartitionSpec as P


def transform_table(slot_harmonic):
    count_all = slot_harmonic.shape[0]
    half_count = count_all // 2
    sine_rows = slot_harmonic > half_count
    harmonic_order = jnp.where(sine_rows, slot_harmonic - half_count, slot_harmonic)
    sector_index = jnp.arange(count_all, dtype=jnp.int32)
    residue = harmonic_order[:, None] * sector_index[None, :] % count_all
    phase_angle = residue.astype(jnp.float32) * jnp.float32(2.0 * math.pi / count_all)
    wave_table = jnp.where(sine_rows[:, None], jnp.sin(phase_angle), jnp.cos(phase_angle))
    single = (slot_harmonic == 0) | (slot_harmonic == half_count)
    weight = jnp.where(single, jnp.float32(1.0 / count_all), jnp.float32(2.0 / count_all))
    return jnp.sqrt(weight)[:, None] * wave_table


def lag_kernel(decay_rates, phase_steps, steps_count):
    lag_value = jnp.arange(steps_count, dtype=jnp.int32).astype(jnp.float32)
    gain_factor = jnp.sqrt(1.0 - jnp.exp(-2.0 * decay_rates))
    return (
        gain_factor[:, None]
        * jnp.exp(-decay_rates[:, None] * lag_value[None, :])
        * jnp.cos(phase_steps[:, None] * lag_value[None, :])
    )


def causal_response(lags, modal):
    steps_count = modal.shape[0]
    padded = jnp.concatenate([jnp.zeros_like(modal), modal], axis=0)
    total = jnp.zeros_like(modal)
    for n in range(steps_count):
        shifted = lax.slice_in_dim(padded, steps_count - n, 2 * steps_count - n, axis=0)
        total = total + lags[:, n][None, :] * shifted
    return total


def local(
    load_history,
    sector_basis,
    harmonic_modes,
    stress_basis,
    mode_decay,
    mode_phase,
    mode_count,
    slot_harmonic,
):
    highest = lax.Precision.HIGHEST
    n_sector = lax.axis_size("sector")
    n_dof = lax.axis_size("dof")
    n_all = n_sector * n_dof
    table = transform_table(slot_harmonic)
    steps_count = load_history.shape[1]
    reduced_count = sector_basis.shape[1]
    piece = steps_count * reduced_count // n_all
    modes_slot = harmonic_modes[0]

    partial_value = jnp.dot(load_history[0], sector_basis, preferred_element_type=jnp.float32)
    sent = partial_value.astype(jnp.bfloat16).reshape(n_all, piece)
    got = lax.all_to_all(sent, ("sector", "dof"), 0, 0, tiled=True)
    reduced = got.reshape(n_sector, n_dof, piece).astype(jnp.float32).sum(axis=1)
    reduced = reduced.astype(jnp.bfloat16).astype(jnp.float32)
    mixed = jnp.dot(table, reduced, precision=highest).astype(jnp.bfloat16)
    sent = jnp.repeat(mixed, n_dof, axis=0)
    spectrum = lax.all_to_all(sent, ("sector", "dof"), 0, 0, tiled=True).reshape(
        steps_count, reduced_count
    )

    live = (jnp.arange(modes_slot.shape[1], dtype=jnp.int32) < mode_count[0]).astype(jnp.float32)
    modal = jnp.dot(spectrum, modes_slot, preferred_element_type=jnp.float32) * live[None, :]
    lags = lag_kernel(mode_decay[0], mode_phase[0], steps_count)
    response = causal_response(lags, modal)
    project_response = response.astype(jnp.bfloat16)
    product = lax.dot_general(
        project_response, modes_slot, (((1,), (1,)), ((), ())), preferred_element_type=jnp.float32
    )
    returned = product.astype(jnp.bfloat16)
    mixed = jnp.einsum(
        "ks,ktc->stc",
        table,
        lax.all_to_all(returned[None], "sector", split_axis=1, concat_axis=0, tiled=True).astype(
            jnp.float32
        ),
        precision=highest,
    )
    back = lax.all_to_all(
        mixed.astype(jnp.bfloat16), "sector", split_axis=0, concat_axis=1, tiled=True
    )[0]
    stress_field = jnp.dot(back, stress_basis, preferred_element_type=jnp.float32).astype(
        jnp.bfloat16
    )
    return stress_field[None]


def solution(mesh):
    return jax.shard_map(
        local,
        mesh=mesh,
        in_specs=(
            P("sector", None, "dof"),
            P("dof", None),
            P("sector", None, None),
            P(None, "dof"),
            P("sector", None),
            P("sector", None),
            P("sector"),
            P(),
        ),
        out_specs=P("sector", None, "dof"),
        check_vma=False,
    )
```

```python
import math

import jax
import jax.numpy as jnp
from jax import lax
from jax.sharding import PartitionSpec as P


def transform_table(slot_harmonic):
    count_all = slot_harmonic.shape[0]
    half_count = count_all // 2
    sine_rows = slot_harmonic > half_count
    harmonic_order = jnp.where(sine_rows, slot_harmonic - half_count, slot_harmonic)
    sector_index = jnp.arange(count_all, dtype=jnp.int32)
    residue = harmonic_order[:, None] * sector_index[None, :] % count_all
    phase_angle = residue.astype(jnp.float32) * jnp.float32(2.0 * math.pi / count_all)
    wave_table = jnp.where(sine_rows[:, None], jnp.sin(phase_angle), jnp.cos(phase_angle))
    single = (slot_harmonic == 0) | (slot_harmonic == half_count)
    weight = jnp.where(single, jnp.float32(1.0 / count_all), jnp.float32(2.0 / count_all))
    return jnp.sqrt(weight)[:, None] * wave_table


def lag_kernel(decay_rates, phase_steps, steps_count):
    lag_value = jnp.arange(steps_count, dtype=jnp.int32).astype(jnp.float32)
    gain_factor = jnp.sqrt(1.0 - jnp.exp(-2.0 * decay_rates))
    return (
        gain_factor[:, None]
        * jnp.exp(-decay_rates[:, None] * lag_value[None, :])
        * jnp.cos(phase_steps[:, None] * lag_value[None, :])
    )


def causal_response(lags, modal):
    steps_count = modal.shape[0]
    padded = jnp.concatenate([jnp.zeros_like(modal), modal], axis=0)
    total = jnp.zeros_like(modal)
    for n in range(steps_count):
        shifted = lax.slice_in_dim(padded, steps_count - n, 2 * steps_count - n, axis=0)
        total = total + lags[:, n][None, :] * shifted
    return total


def local(
    load_history,
    sector_basis,
    harmonic_modes,
    stress_basis,
    mode_decay,
    mode_phase,
    mode_count,
    slot_harmonic,
):
    highest = lax.Precision.HIGHEST
    n_sector = lax.axis_size("sector")
    n_dof = lax.axis_size("dof")
    n_all = n_sector * n_dof
    table = transform_table(slot_harmonic)
    steps_count = load_history.shape[1]
    reduced_count = sector_basis.shape[1]
    piece = steps_count * reduced_count // n_all
    modes_slot = harmonic_modes[0]

    partial_value = jnp.dot(load_history[0], sector_basis, preferred_element_type=jnp.float32)
    sent = partial_value.reshape(n_all, piece)
    got = lax.all_to_all(sent, ("sector", "dof"), 0, 0, tiled=True)
    reduced = got.reshape(n_sector, n_dof, piece).sum(axis=1)
    reduced = reduced.astype(jnp.bfloat16).astype(jnp.float32)
    mixed = jnp.dot(table, reduced, precision=highest).astype(jnp.bfloat16)
    sent = jnp.repeat(mixed, n_dof, axis=0)
    spectrum = lax.all_to_all(sent, ("sector", "dof"), 0, 0, tiled=True).reshape(
        steps_count, reduced_count
    )

    live = (jnp.arange(modes_slot.shape[1], dtype=jnp.int32) < mode_count[0]).astype(jnp.float32)
    modal = jnp.dot(spectrum, modes_slot, preferred_element_type=jnp.float32) * live[None, :]
    lags = lag_kernel(mode_decay[0], mode_phase[0], steps_count)
    response = causal_response(lags, modal)
    project_response = response.astype(jnp.bfloat16)
    product = lax.dot_general(
        project_response, modes_slot, (((1,), (1,)), ((), ())), preferred_element_type=jnp.float32
    )
    returned = product.astype(jnp.bfloat16)
    by_step = lax.all_to_all(returned, "sector", 0, 0, tiled=True).astype(jnp.float32)
    mixed = jnp.dot(table.T, by_step, precision=highest).astype(jnp.bfloat16)
    back = lax.all_to_all(mixed, "sector", 0, 0, tiled=True)
    stress_field = jnp.dot(back, stress_basis, preferred_element_type=jnp.float32).astype(
        jnp.bfloat16
    )
    return stress_field[None]


def solution(mesh):
    return jax.shard_map(
        local,
        mesh=mesh,
        in_specs=(
            P("sector", None, "dof"),
            P("dof", None),
            P("sector", None, None),
            P(None, "dof"),
            P("sector", None),
            P("sector", None),
            P("sector"),
            P(),
        ),
        out_specs=P("sector", None, "dof"),
        check_vma=False,
    )
```

```python
import math

import jax
import jax.numpy as jnp
from jax import lax
from jax.sharding import PartitionSpec as P


def transform_table(slot_harmonic):
    count_all = slot_harmonic.shape[0]
    half_count = count_all // 2
    sine_rows = slot_harmonic > half_count
    harmonic_order = jnp.where(sine_rows, slot_harmonic - half_count, slot_harmonic)
    sector_index = jnp.arange(count_all, dtype=jnp.int32)
    residue = harmonic_order[:, None] * sector_index[None, :] % count_all
    phase_angle = residue.astype(jnp.float32) * jnp.float32(2.0 * math.pi / count_all)
    wave_table = jnp.where(sine_rows[:, None], jnp.sin(phase_angle), jnp.cos(phase_angle))
    single = (slot_harmonic == 0) | (slot_harmonic == half_count)
    weight = jnp.where(single, jnp.float32(1.0 / count_all), jnp.float32(2.0 / count_all))
    return jnp.sqrt(weight)[:, None] * wave_table


def lag_kernel(decay_rates, phase_steps, steps_count):
    lag_value = jnp.arange(steps_count, dtype=jnp.int32).astype(jnp.float32)
    gain_factor = jnp.sqrt(1.0 - jnp.exp(-2.0 * decay_rates))
    return (
        gain_factor[:, None]
        * jnp.exp(-decay_rates[:, None] * lag_value[None, :])
        * jnp.cos(phase_steps[:, None] * lag_value[None, :])
    )


def causal_response(lags, modal):
    steps_count = modal.shape[0]
    padded = jnp.concatenate([jnp.zeros_like(modal), modal], axis=0)
    total = jnp.zeros_like(modal)
    for n in range(steps_count):
        shifted = lax.slice_in_dim(padded, steps_count - n, 2 * steps_count - n, axis=0)
        total = total + lags[:, n][None, :] * shifted
    return total


def local(
    load_history,
    sector_basis,
    harmonic_modes,
    stress_basis,
    mode_decay,
    mode_phase,
    mode_count,
    slot_harmonic,
):
    highest = lax.Precision.HIGHEST
    n_sector = lax.axis_size("sector")
    n_dof = lax.axis_size("dof")
    n_all = n_sector * n_dof
    table = transform_table(slot_harmonic)
    steps_count = load_history.shape[1]
    reduced_count = sector_basis.shape[1]
    piece = steps_count * reduced_count // n_all
    modes_slot = harmonic_modes[0]

    partial_value = jnp.dot(load_history[0], sector_basis, preferred_element_type=jnp.float32)
    sent = partial_value.reshape(n_all, piece)
    got = lax.all_to_all(sent, ("sector", "dof"), 0, 0, tiled=True)
    reduced = got.reshape(n_sector, n_dof, piece).sum(axis=1)
    reduced = reduced.astype(jnp.bfloat16).astype(jnp.float32)
    sent = jnp.dot(jnp.repeat(table, n_dof, axis=0), reduced, precision=highest)
    spectrum = lax.all_to_all(sent, ("sector", "dof"), 0, 0, tiled=True).reshape(
        steps_count, reduced_count
    )

    live = (jnp.arange(modes_slot.shape[1], dtype=jnp.int32) < mode_count[0]).astype(jnp.float32)
    modal = jnp.dot(
        spectrum, modes_slot.astype(jnp.float32), precision=highest
    ) * live[None, :]
    lags = lag_kernel(mode_decay[0], mode_phase[0], steps_count)
    response = causal_response(lags, modal)
    project_response = response.astype(jnp.bfloat16)
    product = lax.dot_general(
        project_response, modes_slot, (((1,), (1,)), ((), ())), preferred_element_type=jnp.float32
    )
    returned = product.astype(jnp.bfloat16)
    by_step = lax.all_to_all(returned, "sector", 0, 0, tiled=True).astype(jnp.float32)
    mixed = jnp.dot(table.T, by_step, precision=highest).astype(jnp.bfloat16)
    back = lax.all_to_all(mixed, "sector", 0, 0, tiled=True)
    stress_field = jnp.dot(back, stress_basis, preferred_element_type=jnp.float32).astype(
        jnp.bfloat16
    )
    return stress_field[None]


def solution(mesh):
    return jax.shard_map(
        local,
        mesh=mesh,
        in_specs=(
            P("sector", None, "dof"),
            P("dof", None),
            P("sector", None, None),
            P(None, "dof"),
            P("sector", None),
            P("sector", None),
            P("sector"),
            P(),
        ),
        out_specs=P("sector", None, "dof"),
        check_vma=False,
    )
```

```python
import math

import jax
import jax.numpy as jnp
from jax import lax
from jax.sharding import PartitionSpec as P


def transform_table(slot_harmonic):
    count_all = slot_harmonic.shape[0]
    half_count = count_all // 2
    sine_rows = slot_harmonic > half_count
    harmonic_order = jnp.where(sine_rows, slot_harmonic - half_count, slot_harmonic)
    sector_index = jnp.arange(count_all, dtype=jnp.int32)
    residue = harmonic_order[:, None] * sector_index[None, :] % count_all
    phase_angle = residue.astype(jnp.float32) * jnp.float32(2.0 * math.pi / count_all)
    wave_table = jnp.where(sine_rows[:, None], jnp.sin(phase_angle), jnp.cos(phase_angle))
    single = (slot_harmonic == 0) | (slot_harmonic == half_count)
    weight = jnp.where(single, jnp.float32(1.0 / count_all), jnp.float32(2.0 / count_all))
    return jnp.sqrt(weight)[:, None] * wave_table


def lag_kernel(decay_rates, phase_steps, steps_count):
    lag_value = jnp.arange(steps_count, dtype=jnp.int32).astype(jnp.float32)
    gain_factor = jnp.sqrt(1.0 - jnp.exp(-2.0 * decay_rates))
    return (
        gain_factor[:, None]
        * jnp.exp(-decay_rates[:, None] * lag_value[None, :])
        * jnp.cos(phase_steps[:, None] * lag_value[None, :])
    )


def causal_response(lags, modal):
    steps_count = modal.shape[0]
    padded = jnp.concatenate([jnp.zeros_like(modal), modal], axis=0)
    total = jnp.zeros_like(modal)
    for n in range(steps_count):
        shifted = lax.slice_in_dim(padded, steps_count - n, 2 * steps_count - n, axis=0)
        total = total + lags[:, n][None, :] * shifted
    return total


def local(
    load_history,
    sector_basis,
    harmonic_modes,
    stress_basis,
    mode_decay,
    mode_phase,
    mode_count,
    slot_harmonic,
):
    highest = lax.Precision.HIGHEST
    n_sector = lax.axis_size("sector")
    n_dof = lax.axis_size("dof")
    n_all = n_sector * n_dof
    table = transform_table(slot_harmonic)
    steps_count = load_history.shape[1]
    reduced_count = sector_basis.shape[1]
    piece = steps_count * reduced_count // n_all
    modes_slot = harmonic_modes[0]

    partial_value = jnp.dot(load_history[0], sector_basis, preferred_element_type=jnp.float32)
    sent = partial_value.reshape(n_all, piece)
    got = lax.all_to_all(sent, ("sector", "dof"), 0, 0, tiled=True)
    wide_table = jnp.repeat(jnp.repeat(table, n_dof, axis=0), n_dof, axis=1)
    sent = jnp.dot(wide_table, got, precision=highest)
    spectrum = lax.all_to_all(sent, ("sector", "dof"), 0, 0, tiled=True).reshape(
        steps_count, reduced_count
    )

    live = (jnp.arange(modes_slot.shape[1], dtype=jnp.int32) < mode_count[0]).astype(jnp.float32)
    modal = jnp.dot(
        spectrum, modes_slot.astype(jnp.float32), precision=highest
    ) * live[None, :]
    lags = lag_kernel(mode_decay[0], mode_phase[0], steps_count)
    response = causal_response(lags, modal)
    project_response = response.astype(jnp.bfloat16)
    product = lax.dot_general(
        project_response, modes_slot, (((1,), (1,)), ((), ())), preferred_element_type=jnp.float32
    )
    returned = product.astype(jnp.bfloat16)
    by_step = lax.all_to_all(returned, "sector", 0, 0, tiled=True).astype(jnp.float32)
    mixed = jnp.dot(table.T, by_step, precision=highest).astype(jnp.bfloat16)
    back = lax.all_to_all(mixed, "sector", 0, 0, tiled=True)
    stress_field = jnp.dot(back, stress_basis, preferred_element_type=jnp.float32).astype(
        jnp.bfloat16
    )
    return stress_field[None]


def solution(mesh):
    return jax.shard_map(
        local,
        mesh=mesh,
        in_specs=(
            P("sector", None, "dof"),
            P("dof", None),
            P("sector", None, None),
            P(None, "dof"),
            P("sector", None),
            P("sector", None),
            P("sector"),
            P(),
        ),
        out_specs=P("sector", None, "dof"),
        check_vma=False,
    )
```

```python
import math

import jax
import jax.numpy as jnp
from jax import lax
from jax.sharding import PartitionSpec as P


def transform_table(slot_harmonic):
    count_all = slot_harmonic.shape[0]
    half_count = count_all // 2
    sine_rows = slot_harmonic > half_count
    harmonic_order = jnp.where(sine_rows, slot_harmonic - half_count, slot_harmonic)
    sector_index = jnp.arange(count_all, dtype=jnp.int32)
    residue = harmonic_order[:, None] * sector_index[None, :] % count_all
    phase_angle = residue.astype(jnp.float32) * jnp.float32(2.0 * math.pi / count_all)
    wave_table = jnp.where(sine_rows[:, None], jnp.sin(phase_angle), jnp.cos(phase_angle))
    single = (slot_harmonic == 0) | (slot_harmonic == half_count)
    weight = jnp.where(single, jnp.float32(1.0 / count_all), jnp.float32(2.0 / count_all))
    return jnp.sqrt(weight)[:, None] * wave_table


def lag_kernel(decay_rates, phase_steps, steps_count):
    lag_value = jnp.arange(steps_count, dtype=jnp.int32).astype(jnp.float32)
    gain_factor = jnp.sqrt(1.0 - jnp.exp(-2.0 * decay_rates))
    return (
        gain_factor[:, None]
        * jnp.exp(-decay_rates[:, None] * lag_value[None, :])
        * jnp.cos(phase_steps[:, None] * lag_value[None, :])
    )


def causal_response(lags, modal):
    steps_count = modal.shape[0]
    padded = jnp.concatenate([jnp.zeros_like(modal), modal], axis=0)
    total = jnp.zeros_like(modal)
    for n in range(steps_count):
        shifted = lax.slice_in_dim(padded, steps_count - n, 2 * steps_count - n, axis=0)
        total = total + lags[:, n][None, :] * shifted
    return total


def local(
    load_history,
    sector_basis,
    harmonic_modes,
    stress_basis,
    mode_decay,
    mode_phase,
    mode_count,
    slot_harmonic,
):
    highest = lax.Precision.HIGHEST
    n_sector = lax.axis_size("sector")
    n_dof = lax.axis_size("dof")
    n_all = n_sector * n_dof
    table = transform_table(slot_harmonic)
    steps_count = load_history.shape[1]
    reduced_count = sector_basis.shape[1]
    piece = steps_count * reduced_count // n_all
    modes_slot = harmonic_modes[0]

    partial_value = jnp.dot(load_history[0], sector_basis, preferred_element_type=jnp.float32)
    sent = partial_value.reshape(n_all, 1, piece)
    got = lax.all_to_all(sent, ("sector", "dof"), 0, 0, tiled=True).reshape(n_all, piece)
    wide_table = jnp.repeat(jnp.repeat(table, n_dof, axis=0), n_dof, axis=1)
    sent = jnp.dot(wide_table, got, precision=highest)
    spectrum = lax.all_to_all(sent, ("sector", "dof"), 0, 0, tiled=True).reshape(
        steps_count, reduced_count
    )

    live = (jnp.arange(modes_slot.shape[1], dtype=jnp.int32) < mode_count[0]).astype(jnp.float32)
    modal = jnp.dot(
        spectrum, modes_slot.astype(jnp.float32), precision=highest
    ) * live[None, :]
    lags = lag_kernel(mode_decay[0], mode_phase[0], steps_count)
    response = causal_response(lags, modal)
    project_response = response.astype(jnp.bfloat16)
    product = lax.dot_general(
        project_response, modes_slot, (((1,), (1,)), ((), ())), preferred_element_type=jnp.float32
    )
    returned = product.astype(jnp.bfloat16)
    halves = (n_sector, 2, reduced_count // 2)
    by_step = lax.all_to_all(returned.reshape(halves), "sector", 0, 0, tiled=True)
    mixed = jnp.einsum(
        "js,jhc->shc", table, by_step.astype(jnp.float32), precision=highest
    ).astype(jnp.bfloat16)
    back = lax.all_to_all(mixed, "sector", 0, 0, tiled=True)
    stress_field = jnp.einsum(
        "thc,hcn->tn", back, stress_basis.reshape(halves[1], halves[2], -1),
        preferred_element_type=jnp.float32,
    ).astype(jnp.bfloat16)
    return stress_field[None]


def solution(mesh):
    return jax.shard_map(
        local,
        mesh=mesh,
        in_specs=(
            P("sector", None, "dof"),
            P("dof", None),
            P("sector", None, None),
            P(None, "dof"),
            P("sector", None),
            P("sector", None),
            P("sector"),
            P(),
        ),
        out_specs=P("sector", None, "dof"),
        check_vma=False,
    )
```

```python
import math

import jax
import jax.numpy as jnp
from jax import lax
from jax.sharding import PartitionSpec as P


def transform_table(slot_harmonic):
    count_all = slot_harmonic.shape[0]
    half_count = count_all // 2
    sine_rows = slot_harmonic > half_count
    harmonic_order = jnp.where(sine_rows, slot_harmonic - half_count, slot_harmonic)
    sector_index = jnp.arange(count_all, dtype=jnp.int32)
    residue = harmonic_order[:, None] * sector_index[None, :] % count_all
    phase_angle = residue.astype(jnp.float32) * jnp.float32(2.0 * math.pi / count_all)
    wave_table = jnp.where(sine_rows[:, None], jnp.sin(phase_angle), jnp.cos(phase_angle))
    single = (slot_harmonic == 0) | (slot_harmonic == half_count)
    weight = jnp.where(single, jnp.float32(1.0 / count_all), jnp.float32(2.0 / count_all))
    return jnp.sqrt(weight)[:, None] * wave_table


def lag_kernel(decay_rates, phase_steps, steps_count):
    lag_value = jnp.arange(steps_count, dtype=jnp.int32).astype(jnp.float32)
    gain_factor = jnp.sqrt(1.0 - jnp.exp(-2.0 * decay_rates))
    return (
        gain_factor[:, None]
        * jnp.exp(-decay_rates[:, None] * lag_value[None, :])
        * jnp.cos(phase_steps[:, None] * lag_value[None, :])
    )


def causal_response(lags, modal):
    steps_count = modal.shape[0]
    padded = jnp.concatenate([jnp.zeros_like(modal), modal], axis=0)
    total = jnp.zeros_like(modal)
    for n in range(steps_count):
        shifted = lax.slice_in_dim(padded, steps_count - n, 2 * steps_count - n, axis=0)
        total = total + lags[:, n][None, :] * shifted
    return total


def local(
    load_history,
    sector_basis,
    harmonic_modes,
    stress_basis,
    mode_decay,
    mode_phase,
    mode_count,
    slot_harmonic,
):
    highest = lax.Precision.HIGHEST
    n_sector = lax.axis_size("sector")
    n_dof = lax.axis_size("dof")
    n_all = n_sector * n_dof
    table = transform_table(slot_harmonic)
    steps_count = load_history.shape[1]
    reduced_count = sector_basis.shape[1]
    piece = steps_count * reduced_count // n_all
    modes_slot = harmonic_modes[0]

    partial_value = jnp.dot(load_history[0], sector_basis, preferred_element_type=jnp.float32)
    sent = partial_value.reshape(n_all, 1, piece)
    got = lax.all_to_all(sent, ("sector", "dof"), 0, 0, tiled=True).reshape(n_all, piece)
    wide_table = jnp.repeat(jnp.repeat(table, n_dof, axis=0), n_dof, axis=1)
    sent = jnp.dot(wide_table, got, precision=highest).astype(jnp.bfloat16)
    sent = sent.reshape(n_all, 2, piece // 2)
    spectrum = lax.all_to_all(sent, ("sector", "dof"), 0, 0, tiled=True).reshape(
        steps_count, reduced_count
    )

    live = (jnp.arange(modes_slot.shape[1], dtype=jnp.int32) < mode_count[0]).astype(jnp.float32)
    modal = jnp.dot(spectrum, modes_slot, preferred_element_type=jnp.float32) * live[None, :]
    lags = lag_kernel(mode_decay[0], mode_phase[0], steps_count)
    response = causal_response(lags, modal)
    project_response = response.astype(jnp.bfloat16)
    product = lax.dot_general(
        project_response, modes_slot, (((1,), (1,)), ((), ())), preferred_element_type=jnp.float32
    )
    returned = product.astype(jnp.bfloat16)
    halves = (n_sector, 2, reduced_count // 2)
    by_step = lax.all_to_all(returned.reshape(halves), "sector", 0, 0, tiled=True)
    mixed = jnp.einsum(
        "js,jhc->shc", table, by_step.astype(jnp.float32), precision=highest
    ).astype(jnp.bfloat16)
    back = lax.all_to_all(mixed, "sector", 0, 0, tiled=True)
    stress_field = jnp.einsum(
        "thc,hcn->tn", back, stress_basis.reshape(halves[1], halves[2], -1),
        preferred_element_type=jnp.float32,
    ).astype(jnp.bfloat16)
    return stress_field[None]


def solution(mesh):
    return jax.shard_map(
        local,
        mesh=mesh,
        in_specs=(
            P("sector", None, "dof"),
            P("dof", None),
            P("sector", None, None),
            P(None, "dof"),
            P("sector", None),
            P("sector", None),
            P("sector"),
            P(),
        ),
        out_specs=P("sector", None, "dof"),
        check_vma=False,
    )
```

```python
import math

import jax
import jax.numpy as jnp
from jax import lax
from jax.sharding import PartitionSpec as P


def transform_table(slot_harmonic):
    count_all = slot_harmonic.shape[0]
    half_count = count_all // 2
    sine_rows = slot_harmonic > half_count
    harmonic_order = jnp.where(sine_rows, slot_harmonic - half_count, slot_harmonic)
    sector_index = jnp.arange(count_all, dtype=jnp.int32)
    residue = harmonic_order[:, None] * sector_index[None, :] % count_all
    phase_angle = residue.astype(jnp.float32) * jnp.float32(2.0 * math.pi / count_all)
    wave_table = jnp.where(sine_rows[:, None], jnp.sin(phase_angle), jnp.cos(phase_angle))
    single = (slot_harmonic == 0) | (slot_harmonic == half_count)
    weight = jnp.where(single, jnp.float32(1.0 / count_all), jnp.float32(2.0 / count_all))
    return jnp.sqrt(weight)[:, None] * wave_table


def lag_kernel(decay_rates, phase_steps, steps_count):
    lag_value = jnp.arange(steps_count, dtype=jnp.int32).astype(jnp.float32)
    gain_factor = jnp.sqrt(1.0 - jnp.exp(-2.0 * decay_rates))
    return (
        gain_factor[:, None]
        * jnp.exp(-decay_rates[:, None] * lag_value[None, :])
        * jnp.cos(phase_steps[:, None] * lag_value[None, :])
    )


def causal_response(lags, modal):
    steps_count = modal.shape[0]
    padded = jnp.concatenate([jnp.zeros_like(modal), modal], axis=0)
    total = jnp.zeros_like(modal)
    for n in range(steps_count):
        shifted = lax.slice_in_dim(padded, steps_count - n, 2 * steps_count - n, axis=0)
        total = total + lags[:, n][None, :] * shifted
    return total


def local(
    load_history,
    sector_basis,
    harmonic_modes,
    stress_basis,
    mode_decay,
    mode_phase,
    mode_count,
    slot_harmonic,
):
    highest = lax.Precision.HIGHEST
    n_sector = lax.axis_size("sector")
    n_dof = lax.axis_size("dof")
    n_all = n_sector * n_dof
    table = transform_table(slot_harmonic)
    steps_count = load_history.shape[1]
    reduced_count = sector_basis.shape[1]
    piece = steps_count * reduced_count // n_all
    modes_slot = harmonic_modes[0]

    partial_value = jnp.dot(load_history[0], sector_basis, preferred_element_type=jnp.float32)
    sent = partial_value.astype(jnp.bfloat16).reshape(n_all, 2, piece // 2)
    got = lax.all_to_all(sent, ("sector", "dof"), 0, 0, tiled=True).reshape(n_all, piece)
    wide_table = jnp.repeat(jnp.repeat(table, n_dof, axis=0), n_dof, axis=1)
    sent = jnp.dot(wide_table, got.astype(jnp.float32), precision=highest).astype(jnp.bfloat16)
    sent = sent.reshape(n_all, 2, piece // 2)
    spectrum = lax.all_to_all(sent, ("sector", "dof"), 0, 0, tiled=True).reshape(
        steps_count, reduced_count
    )

    live = (jnp.arange(modes_slot.shape[1], dtype=jnp.int32) < mode_count[0]).astype(jnp.float32)
    modal = jnp.dot(spectrum, modes_slot, preferred_element_type=jnp.float32) * live[None, :]
    lags = lag_kernel(mode_decay[0], mode_phase[0], steps_count)
    response = causal_response(lags, modal)
    project_response = response.astype(jnp.bfloat16)
    product = lax.dot_general(
        project_response, modes_slot, (((1,), (1,)), ((), ())), preferred_element_type=jnp.float32
    )
    returned = product.astype(jnp.bfloat16)
    halves = (n_sector, 2, reduced_count // 2)
    by_step = lax.all_to_all(returned.reshape(halves), "sector", 0, 0, tiled=True)
    mixed = jnp.einsum(
        "js,jhc->shc", table, by_step.astype(jnp.float32), precision=highest
    ).astype(jnp.bfloat16)
    back = lax.all_to_all(mixed, "sector", 0, 0, tiled=True)
    stress_field = jnp.einsum(
        "thc,hcn->tn", back, stress_basis.reshape(halves[1], halves[2], -1),
        preferred_element_type=jnp.float32,
    ).astype(jnp.bfloat16)
    return stress_field[None]


def solution(mesh):
    return jax.shard_map(
        local,
        mesh=mesh,
        in_specs=(
            P("sector", None, "dof"),
            P("dof", None),
            P("sector", None, None),
            P(None, "dof"),
            P("sector", None),
            P("sector", None),
            P("sector"),
            P(),
        ),
        out_specs=P("sector", None, "dof"),
        check_vma=False,
    )
```

```python
import math

import jax
import jax.numpy as jnp
from jax import lax
from jax.sharding import PartitionSpec as P


def transform_table(slot_harmonic):
    count_all = slot_harmonic.shape[0]
    half_count = count_all // 2
    sine_rows = slot_harmonic > half_count
    harmonic_order = jnp.where(sine_rows, slot_harmonic - half_count, slot_harmonic)
    sector_index = jnp.arange(count_all, dtype=jnp.int32)
    residue = harmonic_order[:, None] * sector_index[None, :] % count_all
    phase_angle = residue.astype(jnp.float32) * jnp.float32(2.0 * math.pi / count_all)
    wave_table = jnp.where(sine_rows[:, None], jnp.sin(phase_angle), jnp.cos(phase_angle))
    single = (slot_harmonic == 0) | (slot_harmonic == half_count)
    weight = jnp.where(single, jnp.float32(1.0 / count_all), jnp.float32(2.0 / count_all))
    return jnp.sqrt(weight)[:, None] * wave_table


def lag_kernel(decay_rates, phase_steps, steps_count):
    lag_value = jnp.arange(steps_count, dtype=jnp.int32).astype(jnp.float32)
    gain_factor = jnp.sqrt(1.0 - jnp.exp(-2.0 * decay_rates))
    return (
        gain_factor[:, None]
        * jnp.exp(-decay_rates[:, None] * lag_value[None, :])
        * jnp.cos(phase_steps[:, None] * lag_value[None, :])
    )


def causal_response(lags, modal):
    steps_count = modal.shape[0]
    padded = jnp.concatenate([jnp.zeros_like(modal), modal], axis=0)
    total = jnp.zeros_like(modal)
    for n in range(steps_count):
        shifted = lax.slice_in_dim(padded, steps_count - n, 2 * steps_count - n, axis=0)
        total = total + lags[:, n][None, :] * shifted
    return total


def local(
    load_history,
    sector_basis,
    harmonic_modes,
    stress_basis,
    mode_decay,
    mode_phase,
    mode_count,
    slot_harmonic,
):
    highest = lax.Precision.HIGHEST
    n_sector = lax.axis_size("sector")
    n_dof = lax.axis_size("dof")
    n_all = n_sector * n_dof
    table = transform_table(slot_harmonic)
    steps_count = load_history.shape[1]
    reduced_count = sector_basis.shape[1]
    piece = steps_count * reduced_count // n_all
    modes_slot = harmonic_modes[0]

    partial_value = jnp.dot(load_history[0], sector_basis, preferred_element_type=jnp.float32)
    sent = partial_value.astype(jnp.bfloat16).reshape(n_all, 2, piece // 2)
    got = lax.all_to_all(sent, ("sector", "dof"), 0, 0, tiled=True).reshape(n_all, piece)
    wide_table = jnp.repeat(table, n_dof, axis=1)
    mixed = jnp.dot(wide_table, got.astype(jnp.float32), precision=highest).astype(jnp.bfloat16)
    sent = jnp.broadcast_to(
        mixed.reshape(n_sector, 1, 2, piece // 2), (n_sector, n_dof, 2, piece // 2)
    ).reshape(n_all, 2, piece // 2)
    spectrum = lax.all_to_all(sent, ("sector", "dof"), 0, 0, tiled=True).reshape(
        steps_count, reduced_count
    )

    live = (jnp.arange(modes_slot.shape[1], dtype=jnp.int32) < mode_count[0]).astype(jnp.float32)
    modal = jnp.dot(spectrum, modes_slot, preferred_element_type=jnp.float32) * live[None, :]
    lags = lag_kernel(mode_decay[0], mode_phase[0], steps_count)
    response = causal_response(lags, modal)
    project_response = response.astype(jnp.bfloat16)
    product = lax.dot_general(
        project_response, modes_slot, (((1,), (1,)), ((), ())), preferred_element_type=jnp.float32
    )
    returned = product.astype(jnp.bfloat16)
    halves = (n_sector, 2, reduced_count // 2)
    by_step = lax.all_to_all(returned.reshape(halves), "sector", 0, 0, tiled=True)
    mixed = jnp.einsum(
        "js,jhc->shc", table, by_step.astype(jnp.float32), precision=highest
    ).astype(jnp.bfloat16)
    back = lax.all_to_all(mixed, "sector", 0, 0, tiled=True)
    stress_field = jnp.einsum(
        "thc,hcn->tn", back, stress_basis.reshape(halves[1], halves[2], -1),
        preferred_element_type=jnp.float32,
    ).astype(jnp.bfloat16)
    return stress_field[None]


def solution(mesh):
    return jax.shard_map(
        local,
        mesh=mesh,
        in_specs=(
            P("sector", None, "dof"),
            P("dof", None),
            P("sector", None, None),
            P(None, "dof"),
            P("sector", None),
            P("sector", None),
            P("sector"),
            P(),
        ),
        out_specs=P("sector", None, "dof"),
        check_vma=False,
    )
```

```python
import math

import jax
import jax.numpy as jnp
from jax import lax
from jax.sharding import PartitionSpec as P


def transform_table(slot_harmonic):
    count_all = slot_harmonic.shape[0]
    half_count = count_all // 2
    sine_rows = slot_harmonic > half_count
    harmonic_order = jnp.where(sine_rows, slot_harmonic - half_count, slot_harmonic)
    sector_index = jnp.arange(count_all, dtype=jnp.int32)
    residue = harmonic_order[:, None] * sector_index[None, :] % count_all
    phase_angle = residue.astype(jnp.float32) * jnp.float32(2.0 * math.pi / count_all)
    wave_table = jnp.where(sine_rows[:, None], jnp.sin(phase_angle), jnp.cos(phase_angle))
    single = (slot_harmonic == 0) | (slot_harmonic == half_count)
    weight = jnp.where(single, jnp.float32(1.0 / count_all), jnp.float32(2.0 / count_all))
    return jnp.sqrt(weight)[:, None] * wave_table


def lag_kernel(decay_rates, phase_steps, steps_count):
    lag_value = jnp.arange(steps_count, dtype=jnp.int32).astype(jnp.float32)
    gain_factor = jnp.sqrt(1.0 - jnp.exp(-2.0 * decay_rates))
    return (
        gain_factor[:, None]
        * jnp.exp(-decay_rates[:, None] * lag_value[None, :])
        * jnp.cos(phase_steps[:, None] * lag_value[None, :])
    )


def causal_response(lags, modal):
    steps_count = modal.shape[0]
    padded = jnp.concatenate([jnp.zeros_like(modal), modal], axis=0)
    total = jnp.zeros_like(modal)
    for n in range(steps_count):
        shifted = lax.slice_in_dim(padded, steps_count - n, 2 * steps_count - n, axis=0)
        total = total + lags[:, n][None, :] * shifted
    return total


def local(
    load_history,
    sector_basis,
    harmonic_modes,
    stress_basis,
    mode_decay,
    mode_phase,
    mode_count,
    slot_harmonic,
):
    highest = lax.Precision.HIGHEST
    n_sector = lax.axis_size("sector")
    n_dof = lax.axis_size("dof")
    n_all = n_sector * n_dof
    table = transform_table(slot_harmonic)
    steps_count = load_history.shape[1]
    reduced_count = sector_basis.shape[1]
    piece = steps_count * reduced_count // n_all
    modes_slot = harmonic_modes[0]

    partial_value = jnp.dot(load_history[0], sector_basis, preferred_element_type=jnp.float32)
    group = ("dof", "sector")
    sent = partial_value.astype(jnp.bfloat16).reshape(n_all, 2, piece // 2)
    got = lax.all_to_all(sent, group, 0, 0, tiled=True).reshape(n_all, piece)
    wide_table = jnp.tile(table, (1, n_dof))
    mixed = jnp.dot(wide_table, got.astype(jnp.float32), precision=highest).astype(jnp.bfloat16)
    sent = jnp.broadcast_to(
        mixed.reshape(1, n_sector, 2, piece // 2), (n_dof, n_sector, 2, piece // 2)
    ).reshape(n_all, 2, piece // 2)
    spectrum = lax.all_to_all(sent, group, 0, 0, tiled=True).reshape(steps_count, reduced_count)

    live = (jnp.arange(modes_slot.shape[1], dtype=jnp.int32) < mode_count[0]).astype(jnp.float32)
    modal = jnp.dot(spectrum, modes_slot, preferred_element_type=jnp.float32) * live[None, :]
    lags = lag_kernel(mode_decay[0], mode_phase[0], steps_count)
    response = causal_response(lags, modal)
    project_response = response.astype(jnp.bfloat16)
    product = lax.dot_general(
        project_response, modes_slot, (((1,), (1,)), ((), ())), preferred_element_type=jnp.float32
    )
    returned = product.astype(jnp.bfloat16)
    halves = (n_sector, 2, reduced_count // 2)
    by_step = lax.all_to_all(returned.reshape(halves), "sector", 0, 0, tiled=True)
    mixed = jnp.einsum(
        "js,jhc->shc", table, by_step.astype(jnp.float32), precision=highest
    ).astype(jnp.bfloat16)
    back = lax.all_to_all(mixed, "sector", 0, 0, tiled=True)
    stress_field = jnp.einsum(
        "thc,hcn->tn", back, stress_basis.reshape(halves[1], halves[2], -1),
        preferred_element_type=jnp.float32,
    ).astype(jnp.bfloat16)
    return stress_field[None]


def solution(mesh):
    return jax.shard_map(
        local,
        mesh=mesh,
        in_specs=(
            P("sector", None, "dof"),
            P("dof", None),
            P("sector", None, None),
            P(None, "dof"),
            P("sector", None),
            P("sector", None),
            P("sector"),
            P(),
        ),
        out_specs=P("sector", None, "dof"),
        check_vma=False,
    )
```

```python
import math

import jax
import jax.numpy as jnp
from jax import lax
from jax.sharding import PartitionSpec as P


def transform_table(slot_harmonic):
    count_all = slot_harmonic.shape[0]
    half_count = count_all // 2
    sine_rows = slot_harmonic > half_count
    harmonic_order = jnp.where(sine_rows, slot_harmonic - half_count, slot_harmonic)
    sector_index = jnp.arange(count_all, dtype=jnp.int32)
    residue = harmonic_order[:, None] * sector_index[None, :] % count_all
    phase_angle = residue.astype(jnp.float32) * jnp.float32(2.0 * math.pi / count_all)
    wave_table = jnp.where(sine_rows[:, None], jnp.sin(phase_angle), jnp.cos(phase_angle))
    single = (slot_harmonic == 0) | (slot_harmonic == half_count)
    weight = jnp.where(single, jnp.float32(1.0 / count_all), jnp.float32(2.0 / count_all))
    return jnp.sqrt(weight)[:, None] * wave_table


def lag_kernel(decay_rates, phase_steps, steps_count):
    lag_value = jnp.arange(steps_count, dtype=jnp.int32).astype(jnp.float32)
    gain_factor = jnp.sqrt(1.0 - jnp.exp(-2.0 * decay_rates))
    return (
        gain_factor[:, None]
        * jnp.exp(-decay_rates[:, None] * lag_value[None, :])
        * jnp.cos(phase_steps[:, None] * lag_value[None, :])
    )


def causal_response(lags, modal):
    steps_count = modal.shape[0]
    padded = jnp.concatenate([jnp.zeros_like(modal), modal], axis=0)
    total = jnp.zeros_like(modal)
    for n in range(steps_count):
        shifted = lax.slice_in_dim(padded, steps_count - n, 2 * steps_count - n, axis=0)
        total = total + lags[:, n][None, :] * shifted
    return total


def local(
    load_history,
    sector_basis,
    harmonic_modes,
    stress_basis,
    mode_decay,
    mode_phase,
    mode_count,
    slot_harmonic,
):
    highest = lax.Precision.HIGHEST
    n_sector = lax.axis_size("sector")
    n_dof = lax.axis_size("dof")
    n_all = n_sector * n_dof
    table = transform_table(slot_harmonic)
    steps_count = load_history.shape[1]
    reduced_count = sector_basis.shape[1]
    piece = steps_count * reduced_count // n_all
    modes_slot = harmonic_modes[0]

    partial_value = jnp.dot(load_history[0], sector_basis, preferred_element_type=jnp.float32)
    sent = partial_value.astype(jnp.bfloat16).reshape(n_all, 3, piece // 3)
    got = lax.all_to_all(sent, ("sector", "dof"), 0, 0, tiled=True).reshape(n_all, piece)
    wide_table = jnp.repeat(table, n_dof, axis=1)
    mixed = jnp.dot(wide_table, got.astype(jnp.float32), precision=highest).astype(jnp.bfloat16)
    sent = jnp.broadcast_to(
        mixed.reshape(n_sector, 1, 3, piece // 3), (n_sector, n_dof, 3, piece // 3)
    ).reshape(n_all, 3, piece // 3)
    spectrum = lax.all_to_all(sent, ("sector", "dof"), 0, 0, tiled=True).reshape(
        steps_count, reduced_count
    )

    live = (jnp.arange(modes_slot.shape[1], dtype=jnp.int32) < mode_count[0]).astype(jnp.float32)
    modal = jnp.dot(spectrum, modes_slot, preferred_element_type=jnp.float32) * live[None, :]
    lags = lag_kernel(mode_decay[0], mode_phase[0], steps_count)
    response = causal_response(lags, modal)
    project_response = response.astype(jnp.bfloat16)
    product = lax.dot_general(
        project_response, modes_slot, (((1,), (1,)), ((), ())), preferred_element_type=jnp.float32
    )
    returned = product.astype(jnp.bfloat16)
    halves = (n_sector, 2, reduced_count // 2)
    by_step = lax.all_to_all(returned.reshape(halves), "sector", 0, 0, tiled=True)
    mixed = jnp.einsum(
        "js,jhc->shc", table, by_step.astype(jnp.float32), precision=highest
    ).astype(jnp.bfloat16)
    back = lax.all_to_all(mixed, "sector", 0, 0, tiled=True)
    stress_field = jnp.einsum(
        "thc,hcn->tn", back, stress_basis.reshape(halves[1], halves[2], -1),
        preferred_element_type=jnp.float32,
    ).astype(jnp.bfloat16)
    return stress_field[None]


def solution(mesh):
    return jax.shard_map(
        local,
        mesh=mesh,
        in_specs=(
            P("sector", None, "dof"),
            P("dof", None),
            P("sector", None, None),
            P(None, "dof"),
            P("sector", None),
            P("sector", None),
            P("sector"),
            P(),
        ),
        out_specs=P("sector", None, "dof"),
        check_vma=False,
    )
```

```python
import math

import jax
import jax.numpy as jnp
from jax import lax
from jax.sharding import PartitionSpec as P


def transform_table(slot_harmonic):
    count_all = slot_harmonic.shape[0]
    half_count = count_all // 2
    sine_rows = slot_harmonic > half_count
    harmonic_order = jnp.where(sine_rows, slot_harmonic - half_count, slot_harmonic)
    sector_index = jnp.arange(count_all, dtype=jnp.int32)
    residue = harmonic_order[:, None] * sector_index[None, :] % count_all
    phase_angle = residue.astype(jnp.float32) * jnp.float32(2.0 * math.pi / count_all)
    wave_table = jnp.where(sine_rows[:, None], jnp.sin(phase_angle), jnp.cos(phase_angle))
    single = (slot_harmonic == 0) | (slot_harmonic == half_count)
    weight = jnp.where(single, jnp.float32(1.0 / count_all), jnp.float32(2.0 / count_all))
    return jnp.sqrt(weight)[:, None] * wave_table


def lag_kernel(decay_rates, phase_steps, steps_count):
    lag_value = jnp.arange(steps_count, dtype=jnp.int32).astype(jnp.float32)
    gain_factor = jnp.sqrt(1.0 - jnp.exp(-2.0 * decay_rates))
    return (
        gain_factor[:, None]
        * jnp.exp(-decay_rates[:, None] * lag_value[None, :])
        * jnp.cos(phase_steps[:, None] * lag_value[None, :])
    )


def causal_response(lags, modal):
    steps_count = modal.shape[0]
    padded = jnp.concatenate([jnp.zeros_like(modal), modal], axis=0)
    total = jnp.zeros_like(modal)
    for n in range(steps_count):
        shifted = lax.slice_in_dim(padded, steps_count - n, 2 * steps_count - n, axis=0)
        total = total + lags[:, n][None, :] * shifted
    return total


def local(
    load_history,
    sector_basis,
    harmonic_modes,
    stress_basis,
    mode_decay,
    mode_phase,
    mode_count,
    slot_harmonic,
):
    highest = lax.Precision.HIGHEST
    n_sector = lax.axis_size("sector")
    n_dof = lax.axis_size("dof")
    n_all = n_sector * n_dof
    table = transform_table(slot_harmonic)
    steps_count = load_history.shape[1]
    reduced_count = sector_basis.shape[1]
    piece = steps_count * reduced_count // n_all
    modes_slot = harmonic_modes[0]

    partial_value = jnp.dot(load_history[0], sector_basis, preferred_element_type=jnp.float32)
    sent = partial_value.astype(jnp.bfloat16).reshape(n_all, 2, piece // 2)
    got = lax.all_to_all(sent, ("sector", "dof"), 0, 0, tiled=True).reshape(n_all, piece)
    wide_table = jnp.repeat(table, n_dof, axis=1)
    mixed = jnp.dot(wide_table, got.astype(jnp.float32), precision=highest).astype(jnp.bfloat16)
    sent = jnp.broadcast_to(
        mixed.reshape(n_sector, 1, 2, piece // 2), (n_sector, n_dof, 2, piece // 2)
    ).reshape(n_all, 2, piece // 2)
    spectrum = lax.all_to_all(sent, ("sector", "dof"), 0, 0, tiled=True).reshape(
        steps_count, reduced_count
    )

    live = (jnp.arange(modes_slot.shape[1], dtype=jnp.int32) < mode_count[0]).astype(jnp.float32)
    modal = jnp.dot(spectrum, modes_slot, preferred_element_type=jnp.float32) * live[None, :]
    lags = lag_kernel(mode_decay[0], mode_phase[0], steps_count)
    response = causal_response(lags, modal)
    project_response = response.astype(jnp.bfloat16)
    product = lax.dot_general(
        project_response, modes_slot, (((1,), (1,)), ((), ())), preferred_element_type=jnp.float32
    )
    returned = product.astype(jnp.bfloat16)
    halves = (n_sector, 2, reduced_count // 2)
    by_step = lax.all_to_all(returned.reshape(halves), "sector", 0, 0, tiled=True)
    back = jnp.einsum(
        "js,jhc->shc", table, by_step.astype(jnp.float32), precision=highest
    ).astype(jnp.bfloat16)
    at_step = jnp.einsum(
        "shc,hcn->sn", back, stress_basis.reshape(halves[1], halves[2], -1),
        preferred_element_type=jnp.float32,
    ).astype(jnp.bfloat16)
    stress_field = lax.all_to_all(
        at_step.reshape(n_sector, 2, -1), "sector", 0, 0, tiled=True
    ).reshape(steps_count, -1)
    return stress_field[None]


def solution(mesh):
    return jax.shard_map(
        local,
        mesh=mesh,
        in_specs=(
            P("sector", None, "dof"),
            P("dof", None),
            P("sector", None, None),
            P(None, "dof"),
            P("sector", None),
            P("sector", None),
            P("sector"),
            P(),
        ),
        out_specs=P("sector", None, "dof"),
        check_vma=False,
    )
```

```python
import math

import jax
import jax.numpy as jnp
from jax import lax
from jax.sharding import PartitionSpec as P


def transform_table(slot_harmonic):
    count_all = slot_harmonic.shape[0]
    half_count = count_all // 2
    sine_rows = slot_harmonic > half_count
    harmonic_order = jnp.where(sine_rows, slot_harmonic - half_count, slot_harmonic)
    sector_index = jnp.arange(count_all, dtype=jnp.int32)
    residue = harmonic_order[:, None] * sector_index[None, :] % count_all
    phase_angle = residue.astype(jnp.float32) * jnp.float32(2.0 * math.pi / count_all)
    wave_table = jnp.where(sine_rows[:, None], jnp.sin(phase_angle), jnp.cos(phase_angle))
    single = (slot_harmonic == 0) | (slot_harmonic == half_count)
    weight = jnp.where(single, jnp.float32(1.0 / count_all), jnp.float32(2.0 / count_all))
    return jnp.sqrt(weight)[:, None] * wave_table


def lag_kernel(decay_rates, phase_steps, steps_count):
    lag_value = jnp.arange(steps_count, dtype=jnp.int32).astype(jnp.float32)
    gain_factor = jnp.sqrt(1.0 - jnp.exp(-2.0 * decay_rates))
    return (
        gain_factor[:, None]
        * jnp.exp(-decay_rates[:, None] * lag_value[None, :])
        * jnp.cos(phase_steps[:, None] * lag_value[None, :])
    )


def causal_response(lags, modal):
    steps_count = modal.shape[0]
    padded = jnp.concatenate([jnp.zeros_like(modal), modal], axis=0)
    total = jnp.zeros_like(modal)
    for n in range(steps_count):
        shifted = lax.slice_in_dim(padded, steps_count - n, 2 * steps_count - n, axis=0)
        total = total + lags[:, n][None, :] * shifted
    return total


def local(
    load_history,
    sector_basis,
    harmonic_modes,
    stress_basis,
    mode_decay,
    mode_phase,
    mode_count,
    slot_harmonic,
):
    highest = lax.Precision.HIGHEST
    n_sector = lax.axis_size("sector")
    n_dof = lax.axis_size("dof")
    n_all = n_sector * n_dof
    table = transform_table(slot_harmonic)
    steps_count = load_history.shape[1]
    reduced_count = sector_basis.shape[1]
    piece = steps_count * reduced_count // n_all
    modes_slot = harmonic_modes[0]

    partial_value = jnp.dot(load_history[0], sector_basis, preferred_element_type=jnp.float32)
    sent = partial_value.astype(jnp.bfloat16).reshape(n_all, 2, piece // 2)
    got = lax.all_to_all(sent, ("sector", "dof"), 0, 0, tiled=True).reshape(n_all, piece)
    wide_table = jnp.repeat(table, n_dof, axis=1)
    mixed = jnp.dot(wide_table, got.astype(jnp.float32), precision=lax.Precision.HIGH).astype(jnp.bfloat16)
    sent = jnp.broadcast_to(
        mixed.reshape(n_sector, 1, 2, piece // 2), (n_sector, n_dof, 2, piece // 2)
    ).reshape(n_all, 2, piece // 2)
    spectrum = lax.all_to_all(sent, ("sector", "dof"), 0, 0, tiled=True).reshape(
        steps_count, reduced_count
    )

    live = (jnp.arange(modes_slot.shape[1], dtype=jnp.int32) < mode_count[0]).astype(jnp.float32)
    modal = jnp.dot(spectrum, modes_slot, preferred_element_type=jnp.float32) * live[None, :]
    lags = lag_kernel(mode_decay[0], mode_phase[0], steps_count)
    response = causal_response(lags, modal)
    project_response = response.astype(jnp.bfloat16)
    product = lax.dot_general(
        project_response, modes_slot, (((1,), (1,)), ((), ())), preferred_element_type=jnp.float32
    )
    returned = product.astype(jnp.bfloat16)
    halves = (n_sector, 2, reduced_count // 2)
    by_step = lax.all_to_all(returned.reshape(halves), "sector", 0, 0, tiled=True)
    mixed = jnp.einsum(
        "js,jhc->shc", table, by_step.astype(jnp.float32), precision=lax.Precision.HIGH
    ).astype(jnp.bfloat16)
    back = lax.all_to_all(mixed, "sector", 0, 0, tiled=True)
    stress_field = jnp.einsum(
        "thc,hcn->tn", back, stress_basis.reshape(halves[1], halves[2], -1),
        preferred_element_type=jnp.float32,
    ).astype(jnp.bfloat16)
    return stress_field[None]


def solution(mesh):
    return jax.shard_map(
        local,
        mesh=mesh,
        in_specs=(
            P("sector", None, "dof"),
            P("dof", None),
            P("sector", None, None),
            P(None, "dof"),
            P("sector", None),
            P("sector", None),
            P("sector"),
            P(),
        ),
        out_specs=P("sector", None, "dof"),
        check_vma=False,
    )
```
